256 devices in a mesh: row: 64 (over x, z, core), rep: 4 (over y).
Axes of the slice: x: 4, y: 4, z: 8, core: 2. Of those that a mesh axis runs over, the one named last changes fastest.
Arguments:
- features: bfloat16 [32768, 128], P(('row', 'rep')), may hold values from -6 to 6
- weight: bfloat16 [128, 256], replicated, may hold values from -0.5 to 0.5
- bias_vector: float32 [256], replicated, may hold values from -3 to 3
- cotangent: bfloat16 [32768, 256], P(('row', 'rep')), may hold values from -6 to 6
- block_tiles: bfloat16 [64, 4, 96, 1, 128, 128], P('row', 'rep'), as said below
- tile_rows: int32 [64, 4, 96, 1], P('row', 'rep'), may hold values from 0 to 3
- tile_columns: int32 [64, 4, 96, 1], P('row', 'rep'), may hold values from 0 to 63
- tile_live: int32 [64, 4, 96, 1], P('row', 'rep'), may hold values from 0 to 1, as said below
Outputs:
- activated: bfloat16 [32768, 256], P(('row', 'rep'))
- grad_features: bfloat16 [32768, 128], P(('row', 'rep'))
- grad_weight: float32 [128, 256], replicated
- grad_bias: float32 [256], replicated
The draws below stay inside these ranges and needn't reach their ends.
Inputs may be any that keep to these rules, and one draw needn't show every extreme that they name: `block_tiles`: A is symmetric: the tile that a live slot puts at block (i, j) is the transpose of the tile that a live slot puts at block (j, i); every block row has a live diagonal tile. `tile_live`: the number of live slots differs from device to device.
All inputs are finite; a program needn't handle non-finite values.
Results may differ from the reference program's by a relative error of at most 0.0095.
Values may be sent and summed in bfloat16 or wider, within the bound.
No kernel may reach another device: no remote copies, remote signals or barrier semaphores. Data moves between devices by JAX's collectives and lax.ppermute only.
A program may use at most 64 MiB of HBM per device.

```python
import math
import jax
import jax.numpy as jnp
from jax import lax

BLOCK = 128
FIN = 128
FOUT = 256
NB = 1
SLOTS = 96
NODES = 32768
N_ROW = 64
N_REP = 4


def block_structure(key):
    nblocks = N_ROW * N_REP * NB
    slot_ids = jnp.arange(SLOTS, dtype=jnp.int32)
    subkeys = jax.random.split(jax.random.fold_in(key, 11), SLOTS)
    orderings = jax.vmap(lambda subkey: jax.random.permutation(subkey, N_ROW))(subkeys).astype(jnp.int32)
    position = jnp.argsort(orderings, axis=1).astype(jnp.int32)
    partner = jnp.take_along_axis(orderings, jnp.bitwise_xor(position, 1), axis=1)
    partner = jnp.where(slot_ids[:, None] == 0, jnp.arange(N_ROW, dtype=jnp.int32)[None, :], partner)
    quarter_flips = jax.random.randint(jax.random.fold_in(key, 12), (SLOTS,), 0, N_REP).astype(jnp.int32)
    quarter_flips = jnp.where(slot_ids == 0, 0, quarter_flips)
    hub_groups = jax.random.randint(jax.random.fold_in(key, 13), (N_ROW,), 0, 8) == 0
    coin_flips = jax.random.randint(jax.random.fold_in(key, 14), (SLOTS, nblocks), 0, 2).astype(jnp.int32)
    group_ids = jnp.arange(N_ROW, dtype=jnp.int32)[:, None, None, None]
    quarter = jnp.arange(N_REP, dtype=jnp.int32)[None, :, None, None]
    slot_grid = slot_ids[None, None, :, None]
    inner_block = jnp.arange(NB, dtype=jnp.int32)[None, None, None, :]
    grid_shape = (N_ROW, N_REP, SLOTS, NB)
    row_quarter = jnp.bitwise_xor(quarter, quarter_flips[slot_grid])
    partner_group = partner[slot_grid, group_ids]
    first_block = (group_ids * N_REP + row_quarter) * NB + inner_block
    second_block = (partner_group * N_REP + quarter) * NB + inner_block
    first_block = jnp.broadcast_to(first_block, grid_shape)
    second_block = jnp.broadcast_to(second_block, grid_shape)
    lower_block = jnp.minimum(first_block, second_block)
    always = (slot_grid == 0) | hub_groups[group_ids] | hub_groups[partner_group]
    live_flags = jnp.where(always, 1, coin_flips[jnp.broadcast_to(slot_grid, grid_shape), lower_block]).astype(jnp.int32)
    row_index = jnp.broadcast_to(row_quarter * NB + inner_block, grid_shape).astype(jnp.int32)
    column_index = jnp.broadcast_to(partner_group * NB + inner_block, grid_shape).astype(jnp.int32)
    return (row_index, column_index, live_flags, first_block, second_block, lower_block)


def draw_tile_rows(key, part):
    return block_structure(key)[0]


def draw_tile_columns(key, part):
    return block_structure(key)[1]


def draw_tile_live(key, part):
    return block_structure(key)[2]


def draw_block_tiles(key, part):
    nblocks = N_ROW * N_REP * NB
    row_index, column_index, live_flags, first_block, second_block, lower_block = block_structure(key)
    magnitude = 2.0 / math.sqrt(SLOTS * BLOCK)

    def one_slot(slot):
        slot_key = jax.random.fold_in(jax.random.fold_in(key, 15), slot)
        values = jax.random.uniform(jax.random.fold_in(slot_key, 1), (nblocks, BLOCK, BLOCK), jnp.float32, 0.3, 1.0)
        present = jax.random.randint(jax.random.fold_in(slot_key, 2), (nblocks, BLOCK, BLOCK), 0, 2).astype(jnp.float32)
        entries = values * present * magnitude
        lower_now = lower_block[:, :, slot, :]
        picked = entries[lower_now]
        flipped = jnp.swapaxes(picked, -1, -2)
        is_lower = (first_block[:, :, slot, :] == lower_now)[..., None, None]
        self_tile = (first_block[:, :, slot, :] == second_block[:, :, slot, :])[..., None, None]
        tile_values = jnp.where(self_tile, picked + flipped, jnp.where(is_lower, picked, flipped))
        return tile_values.astype(jnp.bfloat16)
    stacked = lax.map(one_slot, jnp.arange(SLOTS, dtype=jnp.int32))
    return jnp.moveaxis(stacked, 0, 2)


def block_scale(own_key, shape, pieces, least, high):
    def one(dim, blocks):
        heights = jax.random.uniform(jax.random.fold_in(jax.random.fold_in(own_key, 6), dim), (blocks,), jnp.float32, least / len(pieces), high / len(pieces))
        return jnp.repeat(jnp.exp(heights), shape[dim] // blocks).reshape((-1,) + (1,) * (len(shape) - dim - 1))

    gain = one(*pieces[0])
    for cut in pieces[1:]:
        gain = gain * one(*cut)
    return gain


def normal_values(rng, extent, scale, limit, cuts=(), kind=jnp.bfloat16):
    values = jax.random.normal(rng, extent, jnp.float32) * scale
    if len(cuts) > 0:
        values = block_scale(rng, extent, cuts, -0.22, 0.18) * values
    return jnp.clip(values, min=-limit, max=limit).astype(kind)


def setup_inputs(seed: int = 0) -> dict:
    key_of = jax.random.split(jax.random.key(seed), 9)
    return {
        "features": normal_values(key_of[0], (NODES, FIN), 1.0, 6.0, ((0, 256),)),
        "weight": normal_values(key_of[1], (FIN, FOUT), FIN ** -0.5, 0.5),
        "bias_vector": normal_values(key_of[2], (FOUT,), 0.5, 3.0, (), jnp.float32),
        "cotangent": normal_values(key_of[3], (NODES, FOUT), 1.0, 6.0, ((0, 256),)),
        "block_tiles": draw_block_tiles(jax.random.fold_in(key_of[8], 71), 0),
        "tile_rows": draw_tile_rows(jax.random.fold_in(key_of[8], 71), 0),
        "tile_columns": draw_tile_columns(jax.random.fold_in(key_of[8], 71), 0),
        "tile_live": draw_tile_live(jax.random.fold_in(key_of[8], 71), 0),
    }


def aggregate(block_tiles, tile_rows, tile_columns, tile_live, node_values):
    feat_width = node_values.shape[1]
    group_rows = N_REP * NB
    node_blocks = node_values.reshape(N_ROW, N_REP, NB, BLOCK, feat_width)
    targets = jnp.arange(group_rows, dtype=jnp.int32)

    def per_group(inputs):
        group_tiles, group_rows_idx, group_columns, group_live = inputs
        running = jnp.zeros((group_rows, BLOCK, feat_width), jnp.float32)
        for quarter in range(N_REP):
            quarter_panel = node_blocks[:, quarter].reshape(N_ROW * NB, BLOCK, feat_width)
            picked = quarter_panel[group_columns[quarter].reshape(-1).astype(jnp.int32)]
            tile_values = group_tiles[quarter].reshape(-1, BLOCK, BLOCK).astype(jnp.float32)
            products = jnp.einsum('sij,sjw->siw', tile_values, picked, precision=lax.Precision.HIGHEST)
            placing = (group_rows_idx[quarter].reshape(-1)[:, None] == targets[None, :]).astype(jnp.float32)
            placing = placing * group_live[quarter].reshape(-1)[:, None].astype(jnp.float32)
            running = running + jnp.einsum('sg,siw->giw', placing, products, precision=lax.Precision.HIGHEST)
        return running
    gathered = lax.map(per_group, (block_tiles, tile_rows, tile_columns, tile_live))
    return gathered.reshape(N_ROW * group_rows * BLOCK, feat_width)

def activate(values):
    return jax.nn.gelu(values, approximate=True)

def reference(features, weight, bias_vector, cotangent, block_tiles, tile_rows, tile_columns, tile_live):
    aggregated = aggregate(block_tiles, tile_rows, tile_columns, tile_live, features.astype(jnp.float32))
    weight_wide = weight.astype(jnp.float32)
    hidden = jnp.dot(aggregated, weight_wide, precision=lax.Precision.HIGHEST, preferred_element_type=jnp.float32) + bias_vector
    activated, pullback = jax.vjp(activate, hidden)
    grad_hidden = pullback(cotangent.astype(jnp.float32))[0]
    pulled = jnp.dot(grad_hidden, weight_wide.T, precision=lax.Precision.HIGHEST, preferred_element_type=jnp.float32)
    grad_features = aggregate(block_tiles, tile_rows, tile_columns, tile_live, pulled).astype(jnp.bfloat16)
    factor = 1.0 / jnp.sqrt(jnp.float32(NODES))
    grad_weight = jnp.dot(aggregated.T, grad_hidden, precision=lax.Precision.HIGHEST, preferred_element_type=jnp.float32) * factor
    grad_bias = lax.optimization_barrier(jnp.sum(grad_hidden, axis=0)) * factor
    return (activated.astype(jnp.bfloat16), grad_features, grad_weight, grad_bias)
```

```python
import math

import jax
import jax.numpy as jnp
from jax import lax
from jax.experimental import pallas as pl
from jax.experimental.pallas import tpu as pltpu
from jax.sharding import PartitionSpec as P

SLOT_CHUNK = 16


def _agg_kernel(cols_ref, rows_ref, live_ref, tiles_ref, *rest):
    *panel_refs, out_ref = rest
    step = pl.program_id(0)
    chunk = tiles_ref.shape[0]

    @pl.when(step == 0)
    def _():
        out_ref[...] = jnp.zeros_like(out_ref)

    for k in range(chunk):
        slot = step * chunk + k
        column = cols_ref[slot]
        row = rows_ref[slot]

        @pl.when(live_ref[slot] != 0)
        def _():
            tile = tiles_ref[k]
            acc = jnp.dot(tile, panel_refs[0][column], preferred_element_type=jnp.float32)
            for panel_ref in panel_refs[1:]:
                acc = acc + jnp.dot(tile, panel_ref[column], preferred_element_type=jnp.float32)
            out_ref[row] += acc


def aggregate(tiles, cols, rows, live, panels, group_rows):
    slot_count, tile_size, _ = tiles.shape
    n_blocks, _, width = panels[0].shape
    chunk = math.gcd(slot_count, SLOT_CHUNK)
    grid_spec = pltpu.PrefetchScalarGridSpec(
        num_scalar_prefetch=3,
        grid=(slot_count // chunk,),
        in_specs=[pl.BlockSpec((chunk, tile_size, tile_size), lambda i, *_: (i, 0, 0))]
        + [pl.BlockSpec((n_blocks, tile_size, width), lambda i, *_: (0, 0, 0)) for _ in panels],
        out_specs=pl.BlockSpec((group_rows, tile_size, width), lambda i, *_: (0, 0, 0)),
    )
    return pl.pallas_call(
        _agg_kernel,
        grid_spec=grid_spec,
        out_shape=jax.ShapeDtypeStruct((group_rows, tile_size, width), jnp.float32),
        compiler_params=pltpu.CompilerParams(dimension_semantics=("arbitrary",)),
    )(cols, rows, live, tiles, *panels)


def gather_rows_a2a(block, axis):
    n = lax.axis_size(axis)
    spread = jnp.broadcast_to(block[None], (n,) + block.shape)
    return lax.all_to_all(spread, axis, 0, 0, tiled=False)


def reduce_rep_a2a(parts):
    received = lax.all_to_all(parts, "rep", 0, 0, tiled=False)
    total = received[0]
    for j in range(1, received.shape[0]):
        total = total + received[j]
    return total


def activate(values):
    return jax.nn.gelu(values, approximate=True)


def split_bf16(values):
    high = values.astype(jnp.bfloat16)
    low = (values - high.astype(jnp.float32)).astype(jnp.bfloat16)
    return high, low


def shards(
    features, weight, bias_vector, cotangent, block_tiles, tile_rows, tile_columns, tile_live
):
    tile_size = block_tiles.shape[-1]
    n_rep = lax.axis_size("rep")
    n_row = lax.axis_size("row")
    fin = features.shape[1]
    fout = weight.shape[1]
    node_total = features.shape[0] * n_row * n_rep
    group_rows = n_rep * (features.shape[0] // tile_size)
    slot_count = block_tiles.shape[2] * block_tiles.shape[3]
    tiles = block_tiles.reshape(slot_count, tile_size, tile_size)
    rows = tile_rows.reshape(slot_count)
    cols = tile_columns.reshape(slot_count)
    live = tile_live.reshape(slot_count)
    weight_wide = weight.astype(jnp.float32)

    x_panel = gather_rows_a2a(features.reshape(-1, tile_size, fin), "row")
    x_panel = x_panel.reshape(n_row, tile_size, fin)
    z_parts = aggregate(tiles, cols, rows, live, [x_panel], group_rows)
    z_own = reduce_rep_a2a(z_parts.reshape(n_rep, -1, fin)).reshape(-1, fin)
    hidden = (
        jnp.dot(z_own, weight_wide, precision=lax.Precision.HIGHEST, preferred_element_type=jnp.float32)
        + bias_vector
    )
    activated, pullback = jax.vjp(activate, hidden)
    grad_hidden = pullback(cotangent.astype(jnp.float32))[0]

    joined = jnp.concatenate([z_own, grad_hidden], axis=1)
    joined_all = lax.all_gather(joined, "row", axis=0, tiled=True)
    z_quarter = joined_all[:, :fin]
    dh_quarter = joined_all[:, fin:]
    p_quarter = jnp.dot(
        dh_quarter, weight_wide.T, precision=lax.Precision.HIGHEST, preferred_element_type=jnp.float32
    )
    p_high, p_low = split_bf16(p_quarter.reshape(n_row, tile_size, fin))
    g_parts = aggregate(tiles, cols, rows, live, [p_high, p_low], group_rows)
    grad_features = reduce_rep_a2a(g_parts.reshape(n_rep, -1, fin)).reshape(-1, fin)

    weight_term = lax.dot_general(
        z_quarter,
        dh_quarter,
        (((0,), (0,)), ((), ())),
        precision=lax.Precision.HIGHEST,
        preferred_element_type=jnp.float32,
    )
    bias_term = jnp.sum(dh_quarter, axis=0)
    pad = (-(fin + 1)) % 8
    terms = jnp.concatenate(
        [weight_term, bias_term[None], jnp.zeros((pad, fout), jnp.float32)], axis=0
    )
    spread = jnp.broadcast_to(terms[None], (n_rep,) + terms.shape)
    totals = reduce_rep_a2a(spread)
    factor = 1.0 / math.sqrt(node_total)
    grad_weight = totals[:fin] * factor
    grad_bias = totals[fin] * factor
    return (activated.astype(jnp.bfloat16), grad_features.astype(jnp.bfloat16), grad_weight, grad_bias)


def solution(mesh):
    in_specs = (
        P(("row", "rep"), None),
        P(),
        P(),
        P(("row", "rep"), None),
        P("row", "rep", None, None, None, None),
        P("row", "rep", None, None),
        P("row", "rep", None, None),
        P("row", "rep", None, None),
    )
    out_specs = (P(("row", "rep"), None), P(("row", "rep"), None), P(), P())
    return jax.shard_map(shards, mesh=mesh, in_specs=in_specs, out_specs=out_specs, check_vma=False)
```

```python
import math

import jax
import jax.numpy as jnp
from jax import lax
from jax.experimental import pallas as pl
from jax.experimental.pallas import tpu as pltpu
from jax.sharding import Mesh, PartitionSpec as P

SLOT_CHUNK = 16


def _agg_kernel(cols_ref, rows_ref, live_ref, tiles_ref, *rest):
    *panel_refs, out_ref = rest
    step = pl.program_id(0)
    chunk = tiles_ref.shape[0]

    @pl.when(step == 0)
    def _():
        out_ref[...] = jnp.zeros_like(out_ref)

    for k in range(chunk):
        slot = step * chunk + k
        column = cols_ref[slot]
        row = rows_ref[slot]

        @pl.when(live_ref[slot] != 0)
        def _():
            tile = tiles_ref[k]
            acc = jnp.dot(tile, panel_refs[0][column], preferred_element_type=jnp.float32)
            for panel_ref in panel_refs[1:]:
                acc = acc + jnp.dot(tile, panel_ref[column], preferred_element_type=jnp.float32)
            out_ref[row] += acc


def aggregate(tiles, cols, rows, live, panels, group_rows):
    slot_count, tile_size, _ = tiles.shape
    n_blocks, _, width = panels[0].shape
    chunk = math.gcd(slot_count, SLOT_CHUNK)
    grid_spec = pltpu.PrefetchScalarGridSpec(
        num_scalar_prefetch=3,
        grid=(slot_count // chunk,),
        in_specs=[pl.BlockSpec((chunk, tile_size, tile_size), lambda i, *_: (i, 0, 0))]
        + [pl.BlockSpec((n_blocks, tile_size, width), lambda i, *_: (0, 0, 0)) for _ in panels],
        out_specs=pl.BlockSpec((group_rows, tile_size, width), lambda i, *_: (0, 0, 0)),
    )
    return pl.pallas_call(
        _agg_kernel,
        grid_spec=grid_spec,
        out_shape=jax.ShapeDtypeStruct((group_rows, tile_size, width), jnp.float32),
        compiler_params=pltpu.CompilerParams(dimension_semantics=("arbitrary",)),
    )(cols, rows, live, tiles, *panels)


def gather_a2a(block, axis):
    n = lax.axis_size(axis)
    spread = jnp.broadcast_to(block[None], (n,) + block.shape)
    return lax.all_to_all(spread, axis, 0, 0, tiled=False)


def gather_rows(block):
    return gather_a2a(gather_a2a(gather_a2a(block, "z"), "x"), "core")


def panel_index(cols):
    n_z = lax.axis_size("z")
    n_core = lax.axis_size("core")
    n_x = lax.axis_size("x")
    core = cols % n_core
    z = (cols // n_core) % n_z
    x = cols // (n_core * n_z)
    return (core * n_x + x) * n_z + z


def reduce_rep_a2a(parts):
    received = lax.all_to_all(parts, "rep", 0, 0, tiled=False)
    total = received[0]
    for j in range(1, received.shape[0]):
        total = total + received[j]
    return total


def activate(values):
    return jax.nn.gelu(values, approximate=True)


def split_bf16(values):
    high = values.astype(jnp.bfloat16)
    low = (values - high.astype(jnp.float32)).astype(jnp.bfloat16)
    return high, low


def shards(
    features, weight, bias_vector, cotangent, block_tiles, tile_rows, tile_columns, tile_live
):
    tile_size = block_tiles.shape[-1]
    n_rep = lax.axis_size("rep")
    n_row = lax.axis_size("x") * lax.axis_size("z") * lax.axis_size("core")
    fin = features.shape[1]
    fout = weight.shape[1]
    node_total = features.shape[0] * n_row * n_rep
    group_rows = n_rep * (features.shape[0] // tile_size)
    slot_count = block_tiles.shape[2] * block_tiles.shape[3]
    tiles = block_tiles.reshape(slot_count, tile_size, tile_size)
    rows = tile_rows.reshape(slot_count)
    cols = panel_index(tile_columns.reshape(slot_count))
    live = tile_live.reshape(slot_count)
    weight_wide = weight.astype(jnp.float32)

    x_panel = gather_rows(features.reshape(-1, tile_size, fin))
    x_panel = x_panel.reshape(n_row, tile_size, fin)
    z_parts = aggregate(tiles, cols, rows, live, [x_panel], group_rows)
    z_own = reduce_rep_a2a(z_parts.reshape(n_rep, -1, fin)).reshape(-1, fin)
    hidden = (
        jnp.dot(z_own, weight_wide, precision=lax.Precision.HIGHEST, preferred_element_type=jnp.float32)
        + bias_vector
    )
    activated, pullback = jax.vjp(activate, hidden)
    grad_hidden = pullback(cotangent.astype(jnp.float32))[0]

    joined = jnp.concatenate([z_own, grad_hidden], axis=1)
    joined_all = gather_rows(joined).reshape(-1, joined.shape[1])
    z_quarter = joined_all[:, :fin]
    dh_quarter = joined_all[:, fin:]
    p_quarter = jnp.dot(
        dh_quarter, weight_wide.T, precision=lax.Precision.HIGHEST, preferred_element_type=jnp.float32
    )
    p_high, p_low = split_bf16(p_quarter.reshape(n_row, tile_size, fin))
    g_parts = aggregate(tiles, cols, rows, live, [p_high, p_low], group_rows)
    grad_features = reduce_rep_a2a(g_parts.reshape(n_rep, -1, fin)).reshape(-1, fin)

    weight_term = lax.dot_general(
        z_quarter,
        dh_quarter,
        (((0,), (0,)), ((), ())),
        precision=lax.Precision.HIGHEST,
        preferred_element_type=jnp.float32,
    )
    bias_term = jnp.sum(dh_quarter, axis=0)
    pad = (-(fin + 1)) % 8
    terms = jnp.concatenate(
        [weight_term, bias_term[None], jnp.zeros((pad, fout), jnp.float32)], axis=0
    )
    spread = jnp.broadcast_to(terms[None], (n_rep,) + terms.shape)
    totals = reduce_rep_a2a(spread)
    factor = 1.0 / math.sqrt(node_total)
    grad_weight = totals[:fin] * factor
    grad_bias = totals[fin] * factor
    return (activated.astype(jnp.bfloat16), grad_features.astype(jnp.bfloat16), grad_weight, grad_bias)


def solution(mesh):
    n_row = mesh.shape["row"]
    n_core = 2
    n_z = 8 if n_row % (8 * n_core) == 0 else 1
    fine = Mesh(
        mesh.devices.reshape(n_row // (n_z * n_core), n_z, n_core, mesh.shape["rep"]),
        ("x", "z", "core", "rep"),
    )
    row = ("x", "z", "core")
    in_specs = (
        P((*row, "rep"), None),
        P(),
        P(),
        P((*row, "rep"), None),
        P(row, "rep", None, None, None, None),
        P(row, "rep", None, None),
        P(row, "rep", None, None),
        P(row, "rep", None, None),
    )
    out_specs = (P((*row, "rep"), None), P((*row, "rep"), None), P(), P())
    return jax.shard_map(shards, mesh=fine, in_specs=in_specs, out_specs=out_specs, check_vma=False)
```

```python
import math

import jax
import jax.numpy as jnp
from jax import lax
from jax.experimental import pallas as pl
from jax.experimental.pallas import tpu as pltpu
from jax.sharding import Mesh, PartitionSpec as P

SLOT_CHUNK = 16


def _agg_kernel(cols_ref, rows_ref, live_ref, tiles_ref, *rest):
    *panel_refs, out_ref = rest
    step = pl.program_id(0)
    chunk = tiles_ref.shape[0]

    @pl.when(step == 0)
    def _():
        out_ref[...] = jnp.zeros_like(out_ref)

    for k in range(chunk):
        slot = step * chunk + k
        column = cols_ref[slot]
        row = rows_ref[slot]

        @pl.when(live_ref[slot] != 0)
        def _():
            tile = tiles_ref[k]
            acc = jnp.dot(tile, panel_refs[0][column], preferred_element_type=jnp.float32)
            for panel_ref in panel_refs[1:]:
                acc = acc + jnp.dot(tile, panel_ref[column], preferred_element_type=jnp.float32)
            out_ref[row] += acc


def aggregate(tiles, cols, rows, live, panels, group_rows):
    slot_count, tile_size, _ = tiles.shape
    n_blocks, _, width = panels[0].shape
    chunk = math.gcd(slot_count, SLOT_CHUNK)
    grid_spec = pltpu.PrefetchScalarGridSpec(
        num_scalar_prefetch=3,
        grid=(slot_count // chunk,),
        in_specs=[pl.BlockSpec((chunk, tile_size, tile_size), lambda i, *_: (i, 0, 0))]
        + [pl.BlockSpec((n_blocks, tile_size, width), lambda i, *_: (0, 0, 0)) for _ in panels],
        out_specs=pl.BlockSpec((group_rows, tile_size, width), lambda i, *_: (0, 0, 0)),
    )
    return pl.pallas_call(
        _agg_kernel,
        grid_spec=grid_spec,
        out_shape=jax.ShapeDtypeStruct((group_rows, tile_size, width), jnp.float32),
        compiler_params=pltpu.CompilerParams(dimension_semantics=("arbitrary",)),
    )(cols, rows, live, tiles, *panels)


def gather_a2a(block, axis):
    n = lax.axis_size(axis)
    spread = jnp.broadcast_to(block[None], (n,) + block.shape)
    return lax.all_to_all(spread, axis, 0, 0, tiled=False)


def gather_rows(block):
    return gather_a2a(gather_a2a(gather_a2a(block, "z"), "x"), "core")


def panel_index(cols):
    n_z = lax.axis_size("z")
    n_core = lax.axis_size("core")
    n_x = lax.axis_size("x")
    core = cols % n_core
    z = (cols // n_core) % n_z
    x = cols // (n_core * n_z)
    return (core * n_x + x) * n_z + z


def reduce_rep_a2a(parts):
    received = lax.all_to_all(parts, "rep", 0, 0, tiled=False)
    total = received[0]
    for j in range(1, received.shape[0]):
        total = total + received[j]
    return total


def activate(values):
    return jax.nn.gelu(values, approximate=True)


def split_bf16(values):
    high = values.astype(jnp.bfloat16)
    low = (values - high.astype(jnp.float32)).astype(jnp.bfloat16)
    return high, low


def shards(
    features, weight, bias_vector, cotangent, block_tiles, tile_rows, tile_columns, tile_live
):
    tile_size = block_tiles.shape[-1]
    n_rep = lax.axis_size("rep")
    n_row = lax.axis_size("x") * lax.axis_size("z") * lax.axis_size("core")
    fin = features.shape[1]
    fout = weight.shape[1]
    node_total = features.shape[0] * n_row * n_rep
    group_rows = n_rep * (features.shape[0] // tile_size)
    slot_count = block_tiles.shape[2] * block_tiles.shape[3]
    tiles = block_tiles.reshape(slot_count, tile_size, tile_size)
    rows = tile_rows.reshape(slot_count)
    cols = tile_columns.reshape(slot_count)
    live = tile_live.reshape(slot_count)
    weight_wide = weight.astype(jnp.float32)

    x_panel = gather_rows(features.reshape(-1, tile_size, fin))
    x_panel = x_panel.reshape(n_row, tile_size, fin)
    z_parts = aggregate(tiles, panel_index(cols), rows, live, [x_panel], group_rows)
    z_own = reduce_rep_a2a(z_parts.reshape(n_rep, -1, fin)).reshape(-1, fin)
    hidden = (
        jnp.dot(z_own, weight_wide, precision=lax.Precision.HIGHEST, preferred_element_type=jnp.float32)
        + bias_vector
    )
    activated, pullback = jax.vjp(activate, hidden)
    grad_hidden = pullback(cotangent.astype(jnp.float32))[0]

    joined = jnp.concatenate([z_own, grad_hidden], axis=1)
    joined_all = lax.all_gather(joined, ("x", "z", "core"), axis=0, tiled=True)
    z_quarter = joined_all[:, :fin]
    dh_quarter = joined_all[:, fin:]
    z_high, z_low = split_bf16(z_quarter)
    dh_high, dh_low = split_bf16(dh_quarter)

    def z_t_dot(a, b):
        return lax.dot_general(a, b, (((0,), (0,)), ((), ())), preferred_element_type=jnp.float32)

    weight_term = z_t_dot(z_high, dh_high) + (z_t_dot(z_high, dh_low) + z_t_dot(z_low, dh_high))
    bias_term = jnp.sum(dh_quarter, axis=0)
    pad = (-(fin + 1)) % 8
    terms = jnp.concatenate(
        [weight_term, bias_term[None], jnp.zeros((pad, fout), jnp.float32)], axis=0
    )
    spread = jnp.broadcast_to(terms[None], (n_rep,) + terms.shape)
    totals = reduce_rep_a2a(spread)

    weight_t = weight.T
    p_quarter = jnp.dot(dh_high, weight_t, preferred_element_type=jnp.float32) + jnp.dot(
        dh_low, weight_t, preferred_element_type=jnp.float32
    )
    p_high, p_low = split_bf16(p_quarter.reshape(n_row, tile_size, fin))
    g_parts = aggregate(tiles, cols, rows, live, [p_high, p_low], group_rows)
    grad_features = reduce_rep_a2a(g_parts.reshape(n_rep, -1, fin)).reshape(-1, fin)

    factor = 1.0 / math.sqrt(node_total)
    grad_weight = totals[:fin] * factor
    grad_bias = totals[fin] * factor
    return (activated.astype(jnp.bfloat16), grad_features.astype(jnp.bfloat16), grad_weight, grad_bias)


def solution(mesh):
    n_row = mesh.shape["row"]
    n_core = 2
    n_z = 8 if n_row % (8 * n_core) == 0 else 1
    fine = Mesh(
        mesh.devices.reshape(n_row // (n_z * n_core), n_z, n_core, mesh.shape["rep"]),
        ("x", "z", "core", "rep"),
    )
    row = ("x", "z", "core")
    in_specs = (
        P((*row, "rep"), None),
        P(),
        P(),
        P((*row, "rep"), None),
        P(row, "rep", None, None, None, None),
        P(row, "rep", None, None),
        P(row, "rep", None, None),
        P(row, "rep", None, None),
    )
    out_specs = (P((*row, "rep"), None), P((*row, "rep"), None), P(), P())
    return jax.shard_map(shards, mesh=fine, in_specs=in_specs, out_specs=out_specs, check_vma=False)
```

```python
import math

import jax
import jax.numpy as jnp
from jax import lax
from jax.experimental import pallas as pl
from jax.experimental.pallas import tpu as pltpu
from jax.sharding import Mesh, PartitionSpec as P

SLOT_CHUNK = 16


def _agg_kernel(cols_ref, rows_ref, live_ref, tiles_ref, *rest):
    *panel_refs, out_ref = rest
    step = pl.program_id(0)
    chunk = tiles_ref.shape[0]

    @pl.when(step == 0)
    def _():
        out_ref[...] = jnp.zeros_like(out_ref)

    for k in range(chunk):
        slot = step * chunk + k
        column = cols_ref[slot]
        row = rows_ref[slot]
        tile = tiles_ref[k]
        acc = jnp.dot(tile, panel_refs[0][column], preferred_element_type=jnp.float32)
        for panel_ref in panel_refs[1:]:
            acc = acc + jnp.dot(tile, panel_ref[column], preferred_element_type=jnp.float32)
        out_ref[row] += jnp.where(live_ref[slot] != 0, acc, 0.0)


def aggregate(tiles, cols, rows, live, panels, group_rows):
    slot_count, tile_size, _ = tiles.shape
    n_blocks, _, width = panels[0].shape
    chunk = math.gcd(slot_count, SLOT_CHUNK)
    grid_spec = pltpu.PrefetchScalarGridSpec(
        num_scalar_prefetch=3,
        grid=(slot_count // chunk,),
        in_specs=[pl.BlockSpec((chunk, tile_size, tile_size), lambda i, *_: (i, 0, 0))]
        + [pl.BlockSpec((n_blocks, tile_size, width), lambda i, *_: (0, 0, 0)) for _ in panels],
        out_specs=pl.BlockSpec((group_rows, tile_size, width), lambda i, *_: (0, 0, 0)),
    )
    return pl.pallas_call(
        _agg_kernel,
        grid_spec=grid_spec,
        out_shape=jax.ShapeDtypeStruct((group_rows, tile_size, width), jnp.float32),
        compiler_params=pltpu.CompilerParams(dimension_semantics=("arbitrary",)),
    )(cols, rows, live, tiles, *panels)


def gather_a2a(block, axis):
    n = lax.axis_size(axis)
    spread = jnp.broadcast_to(block[None], (n,) + block.shape)
    return lax.all_to_all(spread, axis, 0, 0, tiled=False)


def gather_rows(block):
    return gather_a2a(gather_a2a(gather_a2a(block, "z"), "x"), "core")


def panel_index(cols):
    n_z = lax.axis_size("z")
    n_core = lax.axis_size("core")
    n_x = lax.axis_size("x")
    core = cols % n_core
    z = (cols // n_core) % n_z
    x = cols // (n_core * n_z)
    return (core * n_x + x) * n_z + z


def reduce_rep_a2a(parts):
    received = lax.all_to_all(parts, "rep", 0, 0, tiled=False)
    total = received[0]
    for j in range(1, received.shape[0]):
        total = total + received[j]
    return total


def activate(values):
    return jax.nn.gelu(values, approximate=True)


def split_bf16(values):
    high = values.astype(jnp.bfloat16)
    low = (values - high.astype(jnp.float32)).astype(jnp.bfloat16)
    return high, low


def shards(
    features, weight, bias_vector, cotangent, block_tiles, tile_rows, tile_columns, tile_live
):
    tile_size = block_tiles.shape[-1]
    n_rep = lax.axis_size("rep")
    n_row = lax.axis_size("x") * lax.axis_size("z") * lax.axis_size("core")
    fin = features.shape[1]
    fout = weight.shape[1]
    node_total = features.shape[0] * n_row * n_rep
    group_rows = n_rep * (features.shape[0] // tile_size)
    slot_count = block_tiles.shape[2] * block_tiles.shape[3]
    tiles = block_tiles.reshape(slot_count, tile_size, tile_size)
    rows = tile_rows.reshape(slot_count)
    cols = tile_columns.reshape(slot_count)
    live = tile_live.reshape(slot_count)
    weight_wide = weight.astype(jnp.float32)

    x_panel = gather_rows(features.reshape(-1, tile_size, fin))
    x_panel = x_panel.reshape(n_row, tile_size, fin)
    z_parts = aggregate(tiles, panel_index(cols), rows, live, [x_panel], group_rows)
    z_own = reduce_rep_a2a(z_parts.reshape(n_rep, -1, fin)).reshape(-1, fin)
    hidden = (
        jnp.dot(z_own, weight_wide, precision=lax.Precision.HIGHEST, preferred_element_type=jnp.float32)
        + bias_vector
    )
    activated, pullback = jax.vjp(activate, hidden)
    grad_hidden = pullback(cotangent.astype(jnp.float32))[0]

    joined = jnp.concatenate([z_own, grad_hidden], axis=1)
    joined_all = lax.all_gather(joined, ("x", "z", "core"), axis=0, tiled=True)
    z_quarter = joined_all[:, :fin]
    dh_quarter = joined_all[:, fin:]
    z_high, z_low = split_bf16(z_quarter)
    dh_high, dh_low = split_bf16(dh_quarter)

    def z_t_dot(a, b):
        return lax.dot_general(a, b, (((0,), (0,)), ((), ())), preferred_element_type=jnp.float32)

    weight_term = z_t_dot(z_high, dh_high) + (z_t_dot(z_high, dh_low) + z_t_dot(z_low, dh_high))
    bias_term = jnp.sum(dh_quarter, axis=0)
    pad = (-(fin + 1)) % 8
    terms = jnp.concatenate(
        [weight_term, bias_term[None], jnp.zeros((pad, fout), jnp.float32)], axis=0
    )
    spread = jnp.broadcast_to(terms[None], (n_rep,) + terms.shape)
    totals = reduce_rep_a2a(spread)

    weight_t = weight.T
    p_quarter = jnp.dot(dh_high, weight_t, preferred_element_type=jnp.float32) + jnp.dot(
        dh_low, weight_t, preferred_element_type=jnp.float32
    )
    p_high, p_low = split_bf16(p_quarter.reshape(n_row, tile_size, fin))
    g_parts = aggregate(tiles, cols, rows, live, [p_high, p_low], group_rows)
    grad_features = reduce_rep_a2a(g_parts.reshape(n_rep, -1, fin)).reshape(-1, fin)

    factor = 1.0 / math.sqrt(node_total)
    grad_weight = totals[:fin] * factor
    grad_bias = totals[fin] * factor
    return (activated.astype(jnp.bfloat16), grad_features.astype(jnp.bfloat16), grad_weight, grad_bias)


def solution(mesh):
    n_row = mesh.shape["row"]
    n_core = 2
    n_z = 8 if n_row % (8 * n_core) == 0 else 1
    fine = Mesh(
        mesh.devices.reshape(n_row // (n_z * n_core), n_z, n_core, mesh.shape["rep"]),
        ("x", "z", "core", "rep"),
    )
    row = ("x", "z", "core")
    in_specs = (
        P((*row, "rep"), None),
        P(),
        P(),
        P((*row, "rep"), None),
        P(row, "rep", None, None, None, None),
        P(row, "rep", None, None),
        P(row, "rep", None, None),
        P(row, "rep", None, None),
    )
    out_specs = (P((*row, "rep"), None), P((*row, "rep"), None), P(), P())
    return jax.shard_map(shards, mesh=fine, in_specs=in_specs, out_specs=out_specs, check_vma=False)
```

```python
import math

import jax
import jax.numpy as jnp
from jax import lax
from jax.experimental import pallas as pl
from jax.experimental.pallas import tpu as pltpu
from jax.sharding import Mesh, PartitionSpec as P

SLOT_CHUNK = 16


def _agg_kernel(cols_ref, rows_ref, live_ref, tiles_ref, *rest):
    *panel_refs, out_ref = rest
    step = pl.program_id(0)
    chunk = tiles_ref.shape[0]

    @pl.when(step == 0)
    def _():
        out_ref[...] = jnp.zeros_like(out_ref)

    for k in range(chunk):
        slot = step * chunk + k
        column = cols_ref[slot]
        row = rows_ref[slot]
        tile = tiles_ref[k]
        acc = jnp.dot(tile, panel_refs[0][column], preferred_element_type=jnp.float32)
        for panel_ref in panel_refs[1:]:
            acc = acc + jnp.dot(tile, panel_ref[column], preferred_element_type=jnp.float32)
        out_ref[row] += jnp.where(live_ref[slot] != 0, acc, 0.0)


def aggregate(tiles, cols, rows, live, panels, group_rows):
    slot_count, tile_size, _ = tiles.shape
    n_blocks, _, width = panels[0].shape
    chunk = math.gcd(slot_count, SLOT_CHUNK)
    grid_spec = pltpu.PrefetchScalarGridSpec(
        num_scalar_prefetch=3,
        grid=(slot_count // chunk,),
        in_specs=[pl.BlockSpec((chunk, tile_size, tile_size), lambda i, *_: (i, 0, 0))]
        + [pl.BlockSpec((n_blocks, tile_size, width), lambda i, *_: (0, 0, 0)) for _ in panels],
        out_specs=pl.BlockSpec((group_rows, tile_size, width), lambda i, *_: (0, 0, 0)),
    )
    return pl.pallas_call(
        _agg_kernel,
        grid_spec=grid_spec,
        out_shape=jax.ShapeDtypeStruct((group_rows, tile_size, width), jnp.float32),
        compiler_params=pltpu.CompilerParams(dimension_semantics=("arbitrary",)),
    )(cols, rows, live, tiles, *panels)


def gather_a2a(block, axis):
    n = lax.axis_size(axis)
    spread = jnp.broadcast_to(block[None], (n,) + block.shape)
    return lax.all_to_all(spread, axis, 0, 0, tiled=False)


def gather_rows(block):
    return gather_a2a(gather_a2a(gather_a2a(block, "z"), "x"), "core")


def panel_index(cols):
    n_z = lax.axis_size("z")
    n_core = lax.axis_size("core")
    n_x = lax.axis_size("x")
    core = cols % n_core
    z = (cols // n_core) % n_z
    x = cols // (n_core * n_z)
    return (core * n_x + x) * n_z + z


def reduce_rep_a2a(parts):
    received = lax.all_to_all(parts, "rep", 0, 0, tiled=False)
    total = received[0]
    for j in range(1, received.shape[0]):
        total = total + received[j]
    return total


def activate(values):
    return jax.nn.gelu(values, approximate=True)


def split_bf16(values):
    high = values.astype(jnp.bfloat16)
    low = (values - high.astype(jnp.float32)).astype(jnp.bfloat16)
    return high, low


def shards(
    features, weight, bias_vector, cotangent, block_tiles, tile_rows, tile_columns, tile_live
):
    tile_size = block_tiles.shape[-1]
    n_rep = lax.axis_size("rep")
    n_row = lax.axis_size("x") * lax.axis_size("z") * lax.axis_size("core")
    fin = features.shape[1]
    fout = weight.shape[1]
    node_total = features.shape[0] * n_row * n_rep
    group_rows = n_rep * (features.shape[0] // tile_size)
    slot_count = block_tiles.shape[2] * block_tiles.shape[3]
    tiles = block_tiles.reshape(slot_count, tile_size, tile_size)
    rows = tile_rows.reshape(slot_count)
    cols = tile_columns.reshape(slot_count)
    live = tile_live.reshape(slot_count)
    weight_wide = weight.astype(jnp.float32)

    cot_quarter = lax.all_gather(cotangent, ("x", "z", "core"), axis=0, tiled=True)

    x_panel = gather_rows(features.reshape(-1, tile_size, fin))
    x_panel = x_panel.reshape(n_row, tile_size, fin)
    z_parts = aggregate(tiles, panel_index(cols), rows, live, [x_panel], group_rows)
    z_own = reduce_rep_a2a(z_parts.reshape(n_rep, -1, fin)).reshape(-1, fin)
    hidden = (
        jnp.dot(z_own, weight_wide, precision=lax.Precision.HIGHEST, preferred_element_type=jnp.float32)
        + bias_vector
    )
    activated = activate(hidden)

    z_quarter = gather_rows(z_own).reshape(-1, fin)
    n_x, n_z, n_core = (lax.axis_size(a) for a in ("x", "z", "core"))
    cot_quarter = cot_quarter.reshape(n_x, n_z, n_core, -1, fout).transpose(2, 0, 1, 3, 4)
    cot_quarter = cot_quarter.reshape(-1, fout)
    zq_high, zq_low = split_bf16(z_quarter)
    hidden_quarter = (
        jnp.dot(zq_high, weight, preferred_element_type=jnp.float32)
        + jnp.dot(zq_low, weight, preferred_element_type=jnp.float32)
        + bias_vector
    )
    _, pullback = jax.vjp(activate, hidden_quarter)
    dh_quarter = pullback(cot_quarter.astype(jnp.float32))[0]
    cols = panel_index(cols)
    z_high, z_low = split_bf16(z_quarter)
    dh_high, dh_low = split_bf16(dh_quarter)

    def z_t_dot(a, b):
        return lax.dot_general(a, b, (((0,), (0,)), ((), ())), preferred_element_type=jnp.float32)

    weight_term = z_t_dot(z_high, dh_high) + (z_t_dot(z_high, dh_low) + z_t_dot(z_low, dh_high))
    bias_term = jnp.sum(dh_quarter, axis=0)
    pad = (-(fin + 1)) % 8
    terms = jnp.concatenate(
        [weight_term, bias_term[None], jnp.zeros((pad, fout), jnp.float32)], axis=0
    )
    spread = jnp.broadcast_to(terms[None], (n_rep,) + terms.shape)
    totals = reduce_rep_a2a(spread)

    weight_t = weight.T
    p_quarter = jnp.dot(dh_high, weight_t, preferred_element_type=jnp.float32) + jnp.dot(
        dh_low, weight_t, preferred_element_type=jnp.float32
    )
    p_high, p_low = split_bf16(p_quarter.reshape(n_row, tile_size, fin))
    g_parts = aggregate(tiles, cols, rows, live, [p_high, p_low], group_rows)
    grad_features = reduce_rep_a2a(g_parts.reshape(n_rep, -1, fin)).reshape(-1, fin)

    factor = 1.0 / math.sqrt(node_total)
    grad_weight = totals[:fin] * factor
    grad_bias = totals[fin] * factor
    return (activated.astype(jnp.bfloat16), grad_features.astype(jnp.bfloat16), grad_weight, grad_bias)


def solution(mesh):
    n_row = mesh.shape["row"]
    n_core = 2
    n_z = 8 if n_row % (8 * n_core) == 0 else 1
    fine = Mesh(
        mesh.devices.reshape(n_row // (n_z * n_core), n_z, n_core, mesh.shape["rep"]),
        ("x", "z", "core", "rep"),
    )
    row = ("x", "z", "core")
    in_specs = (
        P((*row, "rep"), None),
        P(),
        P(),
        P((*row, "rep"), None),
        P(row, "rep", None, None, None, None),
        P(row, "rep", None, None),
        P(row, "rep", None, None),
        P(row, "rep", None, None),
    )
    out_specs = (P((*row, "rep"), None), P((*row, "rep"), None), P(), P())
    return jax.shard_map(shards, mesh=fine, in_specs=in_specs, out_specs=out_specs, check_vma=False)
```

```python
import math

import jax
import jax.numpy as jnp
from jax import lax
from jax.experimental import pallas as pl
from jax.experimental.pallas import tpu as pltpu
from jax.sharding import Mesh, PartitionSpec as P

SLOT_CHUNK = 16


def _agg_kernel(cols_ref, rows_ref, live_ref, tiles_ref, *rest):
    *panel_refs, out_ref = rest
    step = pl.program_id(0)
    chunk = tiles_ref.shape[0]

    @pl.when(step == 0)
    def _():
        out_ref[...] = jnp.zeros_like(out_ref)

    for k in range(chunk):
        slot = step * chunk + k
        column = cols_ref[slot]
        row = rows_ref[slot]
        tile = tiles_ref[k]
        acc = jnp.dot(tile, panel_refs[0][column], preferred_element_type=jnp.float32)
        for panel_ref in panel_refs[1:]:
            acc = acc + jnp.dot(tile, panel_ref[column], preferred_element_type=jnp.float32)
        out_ref[row] += jnp.where(live_ref[slot] != 0, acc, 0.0)


def aggregate(tiles, cols, rows, live, panels, group_rows):
    slot_count, tile_size, _ = tiles.shape
    n_blocks, _, width = panels[0].shape
    chunk = math.gcd(slot_count, SLOT_CHUNK)
    grid_spec = pltpu.PrefetchScalarGridSpec(
        num_scalar_prefetch=3,
        grid=(slot_count // chunk,),
        in_specs=[pl.BlockSpec((chunk, tile_size, tile_size), lambda i, *_: (i, 0, 0))]
        + [pl.BlockSpec((n_blocks, tile_size, width), lambda i, *_: (0, 0, 0)) for _ in panels],
        out_specs=pl.BlockSpec((group_rows, tile_size, width), lambda i, *_: (0, 0, 0)),
    )
    return pl.pallas_call(
        _agg_kernel,
        grid_spec=grid_spec,
        out_shape=jax.ShapeDtypeStruct((group_rows, tile_size, width), jnp.float32),
        compiler_params=pltpu.CompilerParams(dimension_semantics=("arbitrary",)),
    )(cols, rows, live, tiles, *panels)


def gather_a2a(block, axis):
    n = lax.axis_size(axis)
    spread = jnp.broadcast_to(block[None], (n,) + block.shape)
    return lax.all_to_all(spread, axis, 0, 0, tiled=False)


def gather_rows(block):
    return gather_a2a(gather_a2a(gather_a2a(block, "z"), "x"), "core")


def panel_index(cols):
    n_z = lax.axis_size("z")
    n_core = lax.axis_size("core")
    n_x = lax.axis_size("x")
    core = cols % n_core
    z = (cols // n_core) % n_z
    x = cols // (n_core * n_z)
    return (core * n_x + x) * n_z + z


def reduce_rep_a2a(parts):
    received = lax.all_to_all(parts, "rep", 0, 0, tiled=False)
    total = received[0]
    for j in range(1, received.shape[0]):
        total = total + received[j]
    return total


def activate(values):
    return jax.nn.gelu(values, approximate=True)


def split_bf16(values):
    high = values.astype(jnp.bfloat16)
    low = (values - high.astype(jnp.float32)).astype(jnp.bfloat16)
    return high, low


def shards(
    features, weight, bias_vector, cotangent, block_tiles, tile_rows, tile_columns, tile_live
):
    tile_size = block_tiles.shape[-1]
    n_rep = lax.axis_size("rep")
    n_row = lax.axis_size("x") * lax.axis_size("z") * lax.axis_size("core")
    fin = features.shape[1]
    fout = weight.shape[1]
    node_total = features.shape[0] * n_row * n_rep
    group_rows = n_rep * (features.shape[0] // tile_size)
    slot_count = block_tiles.shape[2] * block_tiles.shape[3]
    tiles = block_tiles.reshape(slot_count, tile_size, tile_size)
    rows = tile_rows.reshape(slot_count)
    cols = tile_columns.reshape(slot_count)
    live = tile_live.reshape(slot_count)
    weight_wide = weight.astype(jnp.float32)

    cot_quarter = lax.all_gather(cotangent, ("x", "z", "core"), axis=0, tiled=True)

    x_panel = gather_rows(features.reshape(-1, tile_size, fin))
    x_panel = x_panel.reshape(n_row, tile_size, fin)
    z_parts = aggregate(tiles, panel_index(cols), rows, live, [x_panel], group_rows)
    z_own = reduce_rep_a2a(z_parts.reshape(n_rep, -1, fin)).reshape(-1, fin)
    hidden = (
        jnp.dot(z_own, weight_wide, precision=lax.Precision.HIGHEST, preferred_element_type=jnp.float32)
        + bias_vector
    )
    activated = activate(hidden)

    z_quarter = gather_rows(z_own).reshape(-1, fin)
    n_x, n_z, n_core = (lax.axis_size(a) for a in ("x", "z", "core"))
    cot_quarter = cot_quarter.reshape(n_x, n_z, n_core, -1, fout).transpose(2, 0, 1, 3, 4)
    cot_quarter = cot_quarter.reshape(-1, fout)
    zq_high, zq_low = split_bf16(z_quarter)
    hidden_quarter = (
        jnp.dot(zq_high, weight, preferred_element_type=jnp.float32)
        + jnp.dot(zq_low, weight, preferred_element_type=jnp.float32)
        + bias_vector
    )
    _, pullback = jax.vjp(activate, hidden_quarter)
    dh_quarter = pullback(cot_quarter.astype(jnp.float32))[0]
    cols = panel_index(cols)
    z_high, z_low = split_bf16(z_quarter)
    dh_high, dh_low = split_bf16(dh_quarter)

    def z_t_dot(a, b):
        return lax.dot_general(a, b, (((0,), (0,)), ((), ())), preferred_element_type=jnp.float32)

    weight_term = z_t_dot(z_high, dh_high) + (z_t_dot(z_high, dh_low) + z_t_dot(z_low, dh_high))
    bias_term = jnp.sum(dh_quarter, axis=0)
    pad = (-(fin + 1)) % 8
    terms = jnp.concatenate(
        [weight_term, bias_term[None], jnp.zeros((pad, fout), jnp.float32)], axis=0
    )

    weight_t = weight.T
    p_quarter = jnp.dot(dh_high, weight_t, preferred_element_type=jnp.float32) + jnp.dot(
        dh_low, weight_t, preferred_element_type=jnp.float32
    )
    p_high, p_low = split_bf16(p_quarter.reshape(n_row, tile_size, fin))
    g_parts = aggregate(tiles, cols, rows, live, [p_high, p_low], group_rows)
    spread = jnp.broadcast_to(terms.reshape(1, -1), (n_rep, terms.size))
    both = reduce_rep_a2a(jnp.concatenate([g_parts.reshape(n_rep, -1), spread], axis=1))
    grad_features = both[: g_parts.size // n_rep].reshape(-1, fin)
    totals = both[g_parts.size // n_rep :].reshape(terms.shape)

    factor = 1.0 / math.sqrt(node_total)
    grad_weight = totals[:fin] * factor
    grad_bias = totals[fin] * factor
    return (activated.astype(jnp.bfloat16), grad_features.astype(jnp.bfloat16), grad_weight, grad_bias)


def solution(mesh):
    n_row = mesh.shape["row"]
    n_core = 2
    n_z = 8 if n_row % (8 * n_core) == 0 else 1
    fine = Mesh(
        mesh.devices.reshape(n_row // (n_z * n_core), n_z, n_core, mesh.shape["rep"]),
        ("x", "z", "core", "rep"),
    )
    row = ("x", "z", "core")
    in_specs = (
        P((*row, "rep"), None),
        P(),
        P(),
        P((*row, "rep"), None),
        P(row, "rep", None, None, None, None),
        P(row, "rep", None, None),
        P(row, "rep", None, None),
        P(row, "rep", None, None),
    )
    out_specs = (P((*row, "rep"), None), P((*row, "rep"), None), P(), P())
    return jax.shard_map(shards, mesh=fine, in_specs=in_specs, out_specs=out_specs, check_vma=False)
```

```python
import math

import jax
import jax.numpy as jnp
from jax import lax
from jax.experimental import pallas as pl
from jax.experimental.pallas import tpu as pltpu
from jax.sharding import Mesh, PartitionSpec as P

SLOT_CHUNK = 16


def _agg_kernel(cols_ref, rows_ref, live_ref, tiles_ref, *rest):
    *panel_refs, out_ref = rest
    step = pl.program_id(0)
    chunk = tiles_ref.shape[0]

    @pl.when(step == 0)
    def _():
        out_ref[...] = jnp.zeros_like(out_ref)

    for k in range(chunk):
        slot = step * chunk + k
        column = cols_ref[slot]
        row = rows_ref[slot]
        tile = tiles_ref[k]
        acc = jnp.dot(tile, panel_refs[0][column], preferred_element_type=jnp.float32)
        for panel_ref in panel_refs[1:]:
            acc = acc + jnp.dot(tile, panel_ref[column], preferred_element_type=jnp.float32)
        out_ref[row] += jnp.where(live_ref[slot] != 0, acc, 0.0)


def aggregate(tiles, cols, rows, live, panels, group_rows):
    slot_count, tile_size, _ = tiles.shape
    n_blocks, _, width = panels[0].shape
    chunk = math.gcd(slot_count, SLOT_CHUNK)
    grid_spec = pltpu.PrefetchScalarGridSpec(
        num_scalar_prefetch=3,
        grid=(slot_count // chunk,),
        in_specs=[pl.BlockSpec((chunk, tile_size, tile_size), lambda i, *_: (i, 0, 0))]
        + [pl.BlockSpec((n_blocks, tile_size, width), lambda i, *_: (0, 0, 0)) for _ in panels],
        out_specs=pl.BlockSpec((group_rows, tile_size, width), lambda i, *_: (0, 0, 0)),
    )
    return pl.pallas_call(
        _agg_kernel,
        grid_spec=grid_spec,
        out_shape=jax.ShapeDtypeStruct((group_rows, tile_size, width), jnp.float32),
        compiler_params=pltpu.CompilerParams(dimension_semantics=("arbitrary",)),
    )(cols, rows, live, tiles, *panels)


def gather_a2a(block, axis):
    n = lax.axis_size(axis)
    spread = jnp.broadcast_to(block[None], (n,) + block.shape)
    return lax.all_to_all(spread, axis, 0, 0, tiled=False)


def gather_rows(block):
    return gather_a2a(gather_a2a(gather_a2a(block, "z"), "x"), "core")


def panel_index(cols):
    n_z = lax.axis_size("z")
    n_core = lax.axis_size("core")
    n_x = lax.axis_size("x")
    core = cols % n_core
    z = (cols // n_core) % n_z
    x = cols // (n_core * n_z)
    return (core * n_x + x) * n_z + z


def reduce_rep_a2a(parts):
    received = lax.all_to_all(parts, "rep", 0, 0, tiled=False)
    total = received[0]
    for j in range(1, received.shape[0]):
        total = total + received[j]
    return total


def activate(values):
    return jax.nn.gelu(values, approximate=True)


def split_bf16(values):
    high = values.astype(jnp.bfloat16)
    low = (values - high.astype(jnp.float32)).astype(jnp.bfloat16)
    return high, low


def shards(
    features, weight, bias_vector, cotangent, block_tiles, tile_rows, tile_columns, tile_live
):
    tile_size = block_tiles.shape[-1]
    n_rep = lax.axis_size("rep")
    n_row = lax.axis_size("x") * lax.axis_size("z") * lax.axis_size("core")
    fin = features.shape[1]
    fout = weight.shape[1]
    node_total = features.shape[0] * n_row * n_rep
    group_rows = n_rep * (features.shape[0] // tile_size)
    slot_count = block_tiles.shape[2] * block_tiles.shape[3]
    tiles = block_tiles.reshape(slot_count, tile_size, tile_size)
    rows = tile_rows.reshape(slot_count)
    cols = tile_columns.reshape(slot_count)
    live = tile_live.reshape(slot_count)
    weight_wide = weight.astype(jnp.float32)

    cot_quarter = lax.all_gather(cotangent, ("core", "x", "z"), axis=0, tiled=True)

    x_panel = gather_rows(features.reshape(-1, tile_size, fin))
    x_panel = x_panel.reshape(n_row, tile_size, fin)
    z_parts = aggregate(tiles, panel_index(cols), rows, live, [x_panel], group_rows)
    z_own = reduce_rep_a2a(z_parts.reshape(n_rep, -1, fin)).reshape(-1, fin)
    hidden = (
        jnp.dot(z_own, weight_wide, precision=lax.Precision.HIGHEST, preferred_element_type=jnp.float32)
        + bias_vector
    )
    activated = activate(hidden)

    z_quarter = gather_rows(z_own).reshape(-1, fin)
    zq_high, zq_low = split_bf16(z_quarter)
    hidden_quarter = (
        jnp.dot(zq_high, weight, preferred_element_type=jnp.float32)
        + jnp.dot(zq_low, weight, preferred_element_type=jnp.float32)
        + bias_vector
    )
    _, pullback = jax.vjp(activate, hidden_quarter)
    dh_quarter = pullback(cot_quarter.astype(jnp.float32))[0]
    cols = panel_index(cols)
    z_high, z_low = split_bf16(z_quarter)
    dh_high, dh_low = split_bf16(dh_quarter)

    def z_t_dot(a, b):
        return lax.dot_general(a, b, (((0,), (0,)), ((), ())), preferred_element_type=jnp.float32)

    weight_term = z_t_dot(z_high, dh_high) + (z_t_dot(z_high, dh_low) + z_t_dot(z_low, dh_high))
    bias_term = jnp.sum(dh_quarter, axis=0)
    pad = (-(fin + 1)) % 8
    terms = jnp.concatenate(
        [weight_term, bias_term[None], jnp.zeros((pad, fout), jnp.float32)], axis=0
    )

    weight_t = weight.T
    p_quarter = jnp.dot(dh_high, weight_t, preferred_element_type=jnp.float32) + jnp.dot(
        dh_low, weight_t, preferred_element_type=jnp.float32
    )
    p_high, p_low = split_bf16(p_quarter.reshape(n_row, tile_size, fin))
    g_parts = aggregate(tiles, cols, rows, live, [p_high, p_low], group_rows)
    spread = jnp.broadcast_to(terms.reshape(1, -1), (n_rep, terms.size))
    both = reduce_rep_a2a(jnp.concatenate([g_parts.reshape(n_rep, -1), spread], axis=1))
    grad_features = both[: g_parts.size // n_rep].reshape(-1, fin)
    totals = both[g_parts.size // n_rep :].reshape(terms.shape)

    factor = 1.0 / math.sqrt(node_total)
    grad_weight = totals[:fin] * factor
    grad_bias = totals[fin] * factor
    return (activated.astype(jnp.bfloat16), grad_features.astype(jnp.bfloat16), grad_weight, grad_bias)


def solution(mesh):
    n_row = mesh.shape["row"]
    n_core = 2
    n_z = 8 if n_row % (8 * n_core) == 0 else 1
    fine = Mesh(
        mesh.devices.reshape(n_row // (n_z * n_core), n_z, n_core, mesh.shape["rep"]),
        ("x", "z", "core", "rep"),
    )
    row = ("x", "z", "core")
    in_specs = (
        P((*row, "rep"), None),
        P(),
        P(),
        P((*row, "rep"), None),
        P(row, "rep", None, None, None, None),
        P(row, "rep", None, None),
        P(row, "rep", None, None),
        P(row, "rep", None, None),
    )
    out_specs = (P((*row, "rep"), None), P((*row, "rep"), None), P(), P())
    return jax.shard_map(shards, mesh=fine, in_specs=in_specs, out_specs=out_specs, check_vma=False)
```

```python
import math

import jax
import jax.numpy as jnp
from jax import lax
from jax.experimental import pallas as pl
from jax.experimental.pallas import tpu as pltpu
from jax.sharding import Mesh, PartitionSpec as P


SLOT_CHUNK = 16


def _agg_kernel(cols_ref, rows_ref, live_ref, tiles_ref, *rest):
    *panel_refs, out_ref = rest
    step = pl.program_id(0)
    chunk = tiles_ref.shape[0]

    @pl.when(step == 0)
    def _():
        out_ref[...] = jnp.zeros_like(out_ref)

    for k in range(chunk):
        slot = step * chunk + k
        column = cols_ref[slot]
        row = rows_ref[slot]
        tile = tiles_ref[k]
        acc = jnp.dot(tile, panel_refs[0][column], preferred_element_type=jnp.float32)
        for panel_ref in panel_refs[1:]:
            acc = acc + jnp.dot(tile, panel_ref[column], preferred_element_type=jnp.float32)
        out_ref[row] += jnp.where(live_ref[slot] != 0, acc, 0.0)


def aggregate(tiles, cols, rows, live, panels, group_rows):
    slot_count, tile_size, _ = tiles.shape
    n_blocks, _, width = panels[0].shape
    chunk = math.gcd(slot_count, SLOT_CHUNK)
    grid_spec = pltpu.PrefetchScalarGridSpec(
        num_scalar_prefetch=3,
        grid=(slot_count // chunk,),
        in_specs=[pl.BlockSpec((chunk, tile_size, tile_size), lambda i, *_: (i, 0, 0))]
        + [pl.BlockSpec((n_blocks, tile_size, width), lambda i, *_: (0, 0, 0)) for _ in panels],
        out_specs=pl.BlockSpec((group_rows, tile_size, width), lambda i, *_: (0, 0, 0)),
    )
    return pl.pallas_call(
        _agg_kernel,
        grid_spec=grid_spec,
        out_shape=jax.ShapeDtypeStruct((group_rows, tile_size, width), jnp.float32),
        compiler_params=pltpu.CompilerParams(dimension_semantics=("arbitrary",)),
    )(cols, rows, live, tiles, *panels)


def gather_a2a(block, axis):
    n = lax.axis_size(axis)
    spread = jnp.broadcast_to(block[None], (n,) + block.shape)
    return lax.all_to_all(spread, axis, 0, 0, tiled=False)


def gather_rows(block):
    return gather_a2a(gather_a2a(gather_a2a(block, "z"), "x"), "core")


def panel_index(cols):
    n_z = lax.axis_size("z")
    n_core = lax.axis_size("core")
    n_x = lax.axis_size("x")
    core = cols % n_core
    z = (cols // n_core) % n_z
    x = cols // (n_core * n_z)
    return (core * n_x + x) * n_z + z


def reduce_rep_a2a(parts):
    received = lax.all_to_all(parts, "rep", 0, 0, tiled=False)
    total = received[0]
    for j in range(1, received.shape[0]):
        total = total + received[j]
    return total


def activate(values):
    return jax.nn.gelu(values, approximate=True)


def split_bf16(values):
    high = values.astype(jnp.bfloat16)
    low = (values - high.astype(jnp.float32)).astype(jnp.bfloat16)
    return high, low


def layer(
    features, weight, bias_vector, cotangent, block_tiles, tile_rows, tile_columns, tile_live
):
    tile_size = block_tiles.shape[-1]
    n_rep = lax.axis_size("rep")
    n_row = lax.axis_size("x") * lax.axis_size("z") * lax.axis_size("core")
    fin = features.shape[1]
    fout = weight.shape[1]
    node_total = features.shape[0] * n_row * n_rep
    group_rows = n_rep * (features.shape[0] // tile_size)
    slot_count = block_tiles.shape[2] * block_tiles.shape[3]
    tiles = block_tiles.reshape(slot_count, tile_size, tile_size)
    rows = tile_rows.reshape(slot_count)
    cols = tile_columns.reshape(slot_count)
    live = tile_live.reshape(slot_count)
    weight_wide = weight.astype(jnp.float32)

    cot_quarter = lax.all_gather(cotangent, ("core", "x", "z"), axis=0, tiled=True)

    x_panel = gather_rows(features.reshape(-1, tile_size, fin))
    x_panel = x_panel.reshape(n_row, tile_size, fin)
    z_parts = aggregate(tiles, panel_index(cols), rows, live, [x_panel], group_rows)
    z_own = reduce_rep_a2a(z_parts.reshape(n_rep, -1, fin)).reshape(-1, fin)
    hidden = (
        jnp.dot(z_own, weight_wide, precision=lax.Precision.HIGHEST, preferred_element_type=jnp.float32)
        + bias_vector
    )
    activated = activate(hidden)

    z_quarter = gather_rows(z_own).reshape(-1, fin)
    zq_high, zq_low = split_bf16(z_quarter)
    hidden_quarter = (
        jnp.dot(zq_high, weight, preferred_element_type=jnp.float32)
        + jnp.dot(zq_low, weight, preferred_element_type=jnp.float32)
        + bias_vector
    )
    _, pullback = jax.vjp(activate, hidden_quarter)
    dh_quarter = pullback(cot_quarter.astype(jnp.float32))[0]
    cols = panel_index(cols)
    z_high, z_low = split_bf16(z_quarter)
    dh_high, dh_low = split_bf16(dh_quarter)

    def z_t_dot(a, b):
        return lax.dot_general(a, b, (((0,), (0,)), ((), ())), preferred_element_type=jnp.float32)

    weight_term = z_t_dot(z_high, dh_high) + (z_t_dot(z_high, dh_low) + z_t_dot(z_low, dh_high))
    bias_term = jnp.sum(dh_quarter, axis=0)
    pad = (-(fin + 1)) % 8
    terms = jnp.concatenate(
        [weight_term, bias_term[None], jnp.zeros((pad, fout), jnp.float32)], axis=0
    )

    spread = jnp.broadcast_to(terms[None], (n_rep,) + terms.shape)
    totals = reduce_rep_a2a(spread)

    weight_t = weight.T
    p_quarter = jnp.dot(dh_high, weight_t, preferred_element_type=jnp.float32) + jnp.dot(
        dh_low, weight_t, preferred_element_type=jnp.float32
    )
    p_high, p_low = split_bf16(p_quarter.reshape(n_row, tile_size, fin))
    g_parts = aggregate(tiles, cols, rows, live, [p_high, p_low], group_rows)
    grad_features = reduce_rep_a2a(g_parts.reshape(n_rep, -1, fin)).reshape(-1, fin)

    factor = 1.0 / math.sqrt(node_total)
    grad_weight = totals[:fin] * factor
    grad_bias = totals[fin] * factor
    return (activated.astype(jnp.bfloat16), grad_features.astype(jnp.bfloat16), grad_weight, grad_bias)


def solution(mesh):
    n_row = mesh.shape["row"]
    n_core = 2
    n_z = 8 if n_row % (8 * n_core) == 0 else 1
    fine = Mesh(
        mesh.devices.reshape(n_row // (n_z * n_core), n_z, n_core, mesh.shape["rep"]),
        ("x", "z", "core", "rep"),
    )
    row = ("x", "z", "core")
    in_specs = (
        P((*row, "rep"), None),
        P(),
        P(),
        P((*row, "rep"), None),
        P(row, "rep", None, None, None, None),
        P(row, "rep", None, None),
        P(row, "rep", None, None),
        P(row, "rep", None, None),
    )
    out_specs = (P((*row, "rep"), None), P((*row, "rep"), None), P(), P())
    return jax.shard_map(layer, mesh=fine, in_specs=in_specs, out_specs=out_specs, check_vma=False)
```

```python
import math

import jax
import jax.numpy as jnp
from jax import lax
from jax.experimental import pallas as pl
from jax.experimental.pallas import tpu as pltpu
from jax.sharding import Mesh, PartitionSpec as P

SLOT_CHUNK = 16


def _agg_kernel(cols_ref, rows_ref, live_ref, tiles_ref, *rest):
    *panel_refs, out_ref = rest
    step = pl.program_id(0)
    chunk = tiles_ref.shape[0]

    @pl.when(step == 0)
    def _():
        out_ref[...] = jnp.zeros_like(out_ref)

    for k in range(chunk):
        slot = step * chunk + k
        column = cols_ref[slot]
        row = rows_ref[slot]
        tile = tiles_ref[k]
        acc = jnp.dot(tile, panel_refs[0][column], preferred_element_type=jnp.float32)
        for panel_ref in panel_refs[1:]:
            acc = acc + jnp.dot(tile, panel_ref[column], preferred_element_type=jnp.float32)
        out_ref[row] += jnp.where(live_ref[slot] != 0, acc, 0.0)


def aggregate(tiles, cols, rows, live, panels, group_rows):
    slot_count, tile_size, _ = tiles.shape
    n_blocks, _, width = panels[0].shape
    chunk = math.gcd(slot_count, SLOT_CHUNK)
    grid_spec = pltpu.PrefetchScalarGridSpec(
        num_scalar_prefetch=3,
        grid=(slot_count // chunk,),
        in_specs=[pl.BlockSpec((chunk, tile_size, tile_size), lambda i, *_: (i, 0, 0))]
        + [pl.BlockSpec((n_blocks, tile_size, width), lambda i, *_: (0, 0, 0)) for _ in panels],
        out_specs=pl.BlockSpec((group_rows, tile_size, width), lambda i, *_: (0, 0, 0)),
    )
    return pl.pallas_call(
        _agg_kernel,
        grid_spec=grid_spec,
        out_shape=jax.ShapeDtypeStruct((group_rows, tile_size, width), jnp.float32),
        compiler_params=pltpu.CompilerParams(dimension_semantics=("arbitrary",)),
    )(cols, rows, live, tiles, *panels)


def gather_a2a(block, axis):
    n = lax.axis_size(axis)
    spread = jnp.broadcast_to(block[None], (n,) + block.shape)
    return lax.all_to_all(spread, axis, 0, 0, tiled=False)


def gather_core(block):
    if lax.axis_size("core") != 2:
        return gather_a2a(block, "core")
    other = lax.ppermute(block, "core", [(0, 1), (1, 0)])
    mine = lax.axis_index("core")
    both = jnp.zeros((2,) + block.shape, block.dtype)
    both = lax.dynamic_update_slice_in_dim(both, block[None], mine, 0)
    return lax.dynamic_update_slice_in_dim(both, other[None], 1 - mine, 0)


def gather_rows(block):
    return gather_core(gather_a2a(gather_a2a(block, "z"), "x"))


def panel_index(cols):
    n_z = lax.axis_size("z")
    n_core = lax.axis_size("core")
    n_x = lax.axis_size("x")
    core = cols % n_core
    z = (cols // n_core) % n_z
    x = cols // (n_core * n_z)
    return (core * n_x + x) * n_z + z


def reduce_rep_a2a(parts):
    received = lax.all_to_all(parts, "rep", 0, 0, tiled=False)
    total = received[0]
    for j in range(1, received.shape[0]):
        total = total + received[j]
    return total


def activate(values):
    return jax.nn.gelu(values, approximate=True)


def split_bf16(values):
    high = values.astype(jnp.bfloat16)
    low = (values - high.astype(jnp.float32)).astype(jnp.bfloat16)
    return high, low


def shards(
    features, weight, bias_vector, cotangent, block_tiles, tile_rows, tile_columns, tile_live
):
    tile_size = block_tiles.shape[-1]
    n_rep = lax.axis_size("rep")
    n_row = lax.axis_size("x") * lax.axis_size("z") * lax.axis_size("core")
    fin = features.shape[1]
    fout = weight.shape[1]
    node_total = features.shape[0] * n_row * n_rep
    group_rows = n_rep * (features.shape[0] // tile_size)
    slot_count = block_tiles.shape[2] * block_tiles.shape[3]
    tiles = block_tiles.reshape(slot_count, tile_size, tile_size)
    rows = tile_rows.reshape(slot_count)
    cols = tile_columns.reshape(slot_count)
    live = tile_live.reshape(slot_count)
    weight_wide = weight.astype(jnp.float32)

    cot_quarter = lax.all_gather(cotangent, ("core", "x", "z"), axis=0, tiled=True)

    x_panel = gather_rows(features.reshape(-1, tile_size, fin))
    x_panel = x_panel.reshape(n_row, tile_size, fin)
    z_parts = aggregate(tiles, panel_index(cols), rows, live, [x_panel], group_rows)
    z_own = reduce_rep_a2a(z_parts.reshape(n_rep, -1, fin)).reshape(-1, fin)
    hidden = (
        jnp.dot(z_own, weight_wide, precision=lax.Precision.HIGHEST, preferred_element_type=jnp.float32)
        + bias_vector
    )
    activated = activate(hidden)

    z_quarter = gather_rows(z_own).reshape(-1, fin)
    zq_high, zq_low = split_bf16(z_quarter)
    hidden_quarter = (
        jnp.dot(zq_high, weight, preferred_element_type=jnp.float32)
        + jnp.dot(zq_low, weight, preferred_element_type=jnp.float32)
        + bias_vector
    )
    _, pullback = jax.vjp(activate, hidden_quarter)
    dh_quarter = pullback(cot_quarter.astype(jnp.float32))[0]
    cols = panel_index(cols)
    z_high, z_low = split_bf16(z_quarter)
    dh_high, dh_low = split_bf16(dh_quarter)

    def z_t_dot(a, b):
        return lax.dot_general(a, b, (((0,), (0,)), ((), ())), preferred_element_type=jnp.float32)

    weight_term = z_t_dot(z_high, dh_high) + (z_t_dot(z_high, dh_low) + z_t_dot(z_low, dh_high))
    bias_term = jnp.sum(dh_quarter, axis=0)
    pad = (-(fin + 1)) % 8
    terms = jnp.concatenate(
        [weight_term, bias_term[None], jnp.zeros((pad, fout), jnp.float32)], axis=0
    )

    weight_t = weight.T
    p_quarter = jnp.dot(dh_high, weight_t, preferred_element_type=jnp.float32) + jnp.dot(
        dh_low, weight_t, preferred_element_type=jnp.float32
    )
    p_high, p_low = split_bf16(p_quarter.reshape(n_row, tile_size, fin))
    g_parts = aggregate(tiles, cols, rows, live, [p_high, p_low], group_rows)
    spread = jnp.broadcast_to(terms.reshape(1, -1), (n_rep, terms.size))
    both = reduce_rep_a2a(jnp.concatenate([g_parts.reshape(n_rep, -1), spread], axis=1))
    grad_features = both[: g_parts.size // n_rep].reshape(-1, fin)
    totals = both[g_parts.size // n_rep :].reshape(terms.shape)

    factor = 1.0 / math.sqrt(node_total)
    grad_weight = totals[:fin] * factor
    grad_bias = totals[fin] * factor
    return (activated.astype(jnp.bfloat16), grad_features.astype(jnp.bfloat16), grad_weight, grad_bias)


def solution(mesh):
    n_row = mesh.shape["row"]
    n_core = 2
    n_z = 8 if n_row % (8 * n_core) == 0 else 1
    fine = Mesh(
        mesh.devices.reshape(n_row // (n_z * n_core), n_z, n_core, mesh.shape["rep"]),
        ("x", "z", "core", "rep"),
    )
    row = ("x", "z", "core")
    in_specs = (
        P((*row, "rep"), None),
        P(),
        P(),
        P((*row, "rep"), None),
        P(row, "rep", None, None, None, None),
        P(row, "rep", None, None),
        P(row, "rep", None, None),
        P(row, "rep", None, None),
    )
    out_specs = (P((*row, "rep"), None), P((*row, "rep"), None), P(), P())
    return jax.shard_map(shards, mesh=fine, in_specs=in_specs, out_specs=out_specs, check_vma=False)
```

```python
import math

import jax
import jax.numpy as jnp
from jax import lax
from jax.experimental import pallas as pl
from jax.experimental.pallas import tpu as pltpu
from jax.sharding import Mesh, PartitionSpec as P

SLOT_CHUNK = 16


def _agg_kernel(cols_ref, rows_ref, live_ref, tiles_ref, *rest):
    *panel_refs, out_ref = rest
    step = pl.program_id(0)
    chunk = tiles_ref.shape[0]

    @pl.when(step == 0)
    def _():
        out_ref[...] = jnp.zeros_like(out_ref)

    for k in range(chunk):
        slot = step * chunk + k
        column = cols_ref[slot]
        row = rows_ref[slot]
        tile = tiles_ref[k]
        acc = jnp.dot(tile, panel_refs[0][column], preferred_element_type=jnp.float32)
        for panel_ref in panel_refs[1:]:
            acc = acc + jnp.dot(tile, panel_ref[column], preferred_element_type=jnp.float32)
        out_ref[row] += jnp.where(live_ref[slot] != 0, acc, 0.0)


def aggregate(tiles, cols, rows, live, panels, group_rows):
    slot_count, tile_size, _ = tiles.shape
    n_blocks, _, width = panels[0].shape
    chunk = math.gcd(slot_count, SLOT_CHUNK)
    grid_spec = pltpu.PrefetchScalarGridSpec(
        num_scalar_prefetch=3,
        grid=(slot_count // chunk,),
        in_specs=[pl.BlockSpec((chunk, tile_size, tile_size), lambda i, *_: (i, 0, 0))]
        + [pl.BlockSpec((n_blocks, tile_size, width), lambda i, *_: (0, 0, 0)) for _ in panels],
        out_specs=pl.BlockSpec((group_rows, tile_size, width), lambda i, *_: (0, 0, 0)),
    )
    return pl.pallas_call(
        _agg_kernel,
        grid_spec=grid_spec,
        out_shape=jax.ShapeDtypeStruct((group_rows, tile_size, width), jnp.float32),
        compiler_params=pltpu.CompilerParams(dimension_semantics=("arbitrary",)),
    )(cols, rows, live, tiles, *panels)


def gather_a2a(block, axis):
    n = lax.axis_size(axis)
    spread = jnp.broadcast_to(block[None], (n,) + block.shape)
    return lax.all_to_all(spread, axis, 0, 0, tiled=False)


def gather_core(block):
    if lax.axis_size("core") != 2:
        return gather_a2a(block, "core")
    other = lax.ppermute(block, "core", [(0, 1), (1, 0)])
    mine = lax.axis_index("core")
    both = jnp.zeros((2,) + block.shape, block.dtype)
    both = lax.dynamic_update_slice_in_dim(both, block[None], mine, 0)
    return lax.dynamic_update_slice_in_dim(both, other[None], 1 - mine, 0)


def gather_rows(block):
    return gather_core(gather_a2a(gather_a2a(block, "z"), "x"))


def panel_index(cols):
    n_z = lax.axis_size("z")
    n_core = lax.axis_size("core")
    n_x = lax.axis_size("x")
    core = cols % n_core
    z = (cols // n_core) % n_z
    x = cols // (n_core * n_z)
    return (core * n_x + x) * n_z + z


def reduce_rep_a2a(parts):
    n = parts.shape[0]
    mine = lax.axis_index("rep")
    received = jnp.zeros_like(parts)
    received = lax.dynamic_update_slice_in_dim(
        received, lax.dynamic_slice_in_dim(parts, mine, 1, 0), mine, 0
    )
    for shift in range(1, n):
        outgoing = lax.dynamic_slice_in_dim(parts, (mine + shift) % n, 1, 0)
        incoming = lax.ppermute(outgoing, "rep", [(j, (j + shift) % n) for j in range(n)])
        received = lax.dynamic_update_slice_in_dim(received, incoming, (mine - shift) % n, 0)
    total = received[0]
    for j in range(1, received.shape[0]):
        total = total + received[j]
    return total


def activate(values):
    return jax.nn.gelu(values, approximate=True)


def split_bf16(values):
    high = values.astype(jnp.bfloat16)
    low = (values - high.astype(jnp.float32)).astype(jnp.bfloat16)
    return high, low


def shards(
    features, weight, bias_vector, cotangent, block_tiles, tile_rows, tile_columns, tile_live
):
    tile_size = block_tiles.shape[-1]
    n_rep = lax.axis_size("rep")
    n_row = lax.axis_size("x") * lax.axis_size("z") * lax.axis_size("core")
    fin = features.shape[1]
    fout = weight.shape[1]
    node_total = features.shape[0] * n_row * n_rep
    group_rows = n_rep * (features.shape[0] // tile_size)
    slot_count = block_tiles.shape[2] * block_tiles.shape[3]
    tiles = block_tiles.reshape(slot_count, tile_size, tile_size)
    rows = tile_rows.reshape(slot_count)
    cols = tile_columns.reshape(slot_count)
    live = tile_live.reshape(slot_count)
    weight_wide = weight.astype(jnp.float32)

    cot_quarter = lax.all_gather(cotangent, ("core", "x", "z"), axis=0, tiled=True)

    x_panel = gather_rows(features.reshape(-1, tile_size, fin))
    x_panel = x_panel.reshape(n_row, tile_size, fin)
    z_parts = aggregate(tiles, panel_index(cols), rows, live, [x_panel], group_rows)
    z_own = reduce_rep_a2a(z_parts.reshape(n_rep, -1, fin)).reshape(-1, fin)
    hidden = (
        jnp.dot(z_own, weight_wide, precision=lax.Precision.HIGHEST, preferred_element_type=jnp.float32)
        + bias_vector
    )
    activated = activate(hidden)

    z_quarter = gather_rows(z_own).reshape(-1, fin)
    zq_high, zq_low = split_bf16(z_quarter)
    hidden_quarter = (
        jnp.dot(zq_high, weight, preferred_element_type=jnp.float32)
        + jnp.dot(zq_low, weight, preferred_element_type=jnp.float32)
        + bias_vector
    )
    _, pullback = jax.vjp(activate, hidden_quarter)
    dh_quarter = pullback(cot_quarter.astype(jnp.float32))[0]
    cols = panel_index(cols)
    z_high, z_low = split_bf16(z_quarter)
    dh_high, dh_low = split_bf16(dh_quarter)

    def z_t_dot(a, b):
        return lax.dot_general(a, b, (((0,), (0,)), ((), ())), preferred_element_type=jnp.float32)

    weight_term = z_t_dot(z_high, dh_high) + (z_t_dot(z_high, dh_low) + z_t_dot(z_low, dh_high))
    bias_term = jnp.sum(dh_quarter, axis=0)
    pad = (-(fin + 1)) % 8
    terms = jnp.concatenate(
        [weight_term, bias_term[None], jnp.zeros((pad, fout), jnp.float32)], axis=0
    )

    weight_t = weight.T
    p_quarter = jnp.dot(dh_high, weight_t, preferred_element_type=jnp.float32) + jnp.dot(
        dh_low, weight_t, preferred_element_type=jnp.float32
    )
    p_high, p_low = split_bf16(p_quarter.reshape(n_row, tile_size, fin))
    g_parts = aggregate(tiles, cols, rows, live, [p_high, p_low], group_rows)
    spread = jnp.broadcast_to(terms.reshape(1, -1), (n_rep, terms.size))
    both = reduce_rep_a2a(jnp.concatenate([g_parts.reshape(n_rep, -1), spread], axis=1))
    grad_features = both[: g_parts.size // n_rep].reshape(-1, fin)
    totals = both[g_parts.size // n_rep :].reshape(terms.shape)

    factor = 1.0 / math.sqrt(node_total)
    grad_weight = totals[:fin] * factor
    grad_bias = totals[fin] * factor
    return (activated.astype(jnp.bfloat16), grad_features.astype(jnp.bfloat16), grad_weight, grad_bias)


def solution(mesh):
    n_row = mesh.shape["row"]
    n_core = 2
    n_z = 8 if n_row % (8 * n_core) == 0 else 1
    fine = Mesh(
        mesh.devices.reshape(n_row // (n_z * n_core), n_z, n_core, mesh.shape["rep"]),
        ("x", "z", "core", "rep"),
    )
    row = ("x", "z", "core")
    in_specs = (
        P((*row, "rep"), None),
        P(),
        P(),
        P((*row, "rep"), None),
        P(row, "rep", None, None, None, None),
        P(row, "rep", None, None),
        P(row, "rep", None, None),
        P(row, "rep", None, None),
    )
    out_specs = (P((*row, "rep"), None), P((*row, "rep"), None), P(), P())
    return jax.shard_map(shards, mesh=fine, in_specs=in_specs, out_specs=out_specs, check_vma=False)
```

```python
import math

import jax
import jax.numpy as jnp
from jax import lax
from jax.experimental import pallas as pl
from jax.experimental.pallas import tpu as pltpu
from jax.sharding import Mesh, PartitionSpec as P

SLOT_CHUNK = 32


def _agg_kernel(cols_ref, rows_ref, live_ref, tiles_ref, *rest):
    *panel_refs, out_ref = rest
    step = pl.program_id(0)
    chunk = tiles_ref.shape[0]

    @pl.when(step == 0)
    def _():
        out_ref[...] = jnp.zeros_like(out_ref)

    for k in range(chunk):
        slot = step * chunk + k
        column = cols_ref[slot]
        row = rows_ref[slot]
        tile = tiles_ref[k]
        acc = jnp.dot(tile, panel_refs[0][column], preferred_element_type=jnp.float32)
        for panel_ref in panel_refs[1:]:
            acc = acc + jnp.dot(tile, panel_ref[column], preferred_element_type=jnp.float32)
        out_ref[row] += jnp.where(live_ref[slot] != 0, acc, 0.0)


def aggregate(tiles, cols, rows, live, panels, group_rows):
    slot_count, tile_size, _ = tiles.shape
    n_blocks, _, width = panels[0].shape
    chunk = math.gcd(slot_count, SLOT_CHUNK)
    grid_spec = pltpu.PrefetchScalarGridSpec(
        num_scalar_prefetch=3,
        grid=(slot_count // chunk,),
        in_specs=[pl.BlockSpec((chunk, tile_size, tile_size), lambda i, *_: (i, 0, 0))]
        + [pl.BlockSpec((n_blocks, tile_size, width), lambda i, *_: (0, 0, 0)) for _ in panels],
        out_specs=pl.BlockSpec((group_rows, tile_size, width), lambda i, *_: (0, 0, 0)),
    )
    return pl.pallas_call(
        _agg_kernel,
        grid_spec=grid_spec,
        out_shape=jax.ShapeDtypeStruct((group_rows, tile_size, width), jnp.float32),
        compiler_params=pltpu.CompilerParams(dimension_semantics=("arbitrary",)),
    )(cols, rows, live, tiles, *panels)


def gather_a2a(block, axis):
    n = lax.axis_size(axis)
    spread = jnp.broadcast_to(block[None], (n,) + block.shape)
    return lax.all_to_all(spread, axis, 0, 0, tiled=False)


def gather_core(block):
    if lax.axis_size("core") != 2:
        return gather_a2a(block, "core")
    other = lax.ppermute(block, "core", [(0, 1), (1, 0)])
    mine = lax.axis_index("core")
    both = jnp.zeros((2,) + block.shape, block.dtype)
    both = lax.dynamic_update_slice_in_dim(both, block[None], mine, 0)
    return lax.dynamic_update_slice_in_dim(both, other[None], 1 - mine, 0)


def gather_rows(block):
    return gather_core(gather_a2a(gather_a2a(block, "z"), "x"))


def panel_index(cols):
    n_z = lax.axis_size("z")
    n_core = lax.axis_size("core")
    n_x = lax.axis_size("x")
    core = cols % n_core
    z = (cols // n_core) % n_z
    x = cols // (n_core * n_z)
    return (core * n_x + x) * n_z + z


def reduce_rep_a2a(parts):
    received = lax.all_to_all(parts, "rep", 0, 0, tiled=False)
    total = received[0]
    for j in range(1, received.shape[0]):
        total = total + received[j]
    return total


def activate(values):
    return jax.nn.gelu(values, approximate=True)


def split_bf16(values):
    high = values.astype(jnp.bfloat16)
    low = (values - high.astype(jnp.float32)).astype(jnp.bfloat16)
    return high, low


def shards(
    features, weight, bias_vector, cotangent, block_tiles, tile_rows, tile_columns, tile_live
):
    tile_size = block_tiles.shape[-1]
    n_rep = lax.axis_size("rep")
    n_row = lax.axis_size("x") * lax.axis_size("z") * lax.axis_size("core")
    fin = features.shape[1]
    fout = weight.shape[1]
    node_total = features.shape[0] * n_row * n_rep
    group_rows = n_rep * (features.shape[0] // tile_size)
    slot_count = block_tiles.shape[2] * block_tiles.shape[3]
    tiles = block_tiles.reshape(slot_count, tile_size, tile_size)
    rows = tile_rows.reshape(slot_count)
    cols = tile_columns.reshape(slot_count)
    live = tile_live.reshape(slot_count)
    weight_wide = weight.astype(jnp.float32)

    cot_quarter = lax.all_gather(cotangent, ("core", "x", "z"), axis=0, tiled=True)

    x_panel = gather_rows(features.reshape(-1, tile_size, fin))
    x_panel = x_panel.reshape(n_row, tile_size, fin)
    z_parts = aggregate(tiles, panel_index(cols), rows, live, [x_panel], group_rows)
    z_own = reduce_rep_a2a(z_parts.reshape(n_rep, -1, fin)).reshape(-1, fin)
    hidden = (
        jnp.dot(z_own, weight_wide, precision=lax.Precision.HIGHEST, preferred_element_type=jnp.float32)
        + bias_vector
    )
    activated = activate(hidden)

    z_quarter = gather_rows(z_own).reshape(-1, fin)
    zq_high, zq_low = split_bf16(z_quarter)
    hidden_quarter = (
        jnp.dot(zq_high, weight, preferred_element_type=jnp.float32)
        + jnp.dot(zq_low, weight, preferred_element_type=jnp.float32)
        + bias_vector
    )
    _, pullback = jax.vjp(activate, hidden_quarter)
    dh_quarter = pullback(cot_quarter.astype(jnp.float32))[0]
    cols = panel_index(cols)
    z_high, z_low = split_bf16(z_quarter)
    dh_high, dh_low = split_bf16(dh_quarter)

    def z_t_dot(a, b):
        return lax.dot_general(a, b, (((0,), (0,)), ((), ())), preferred_element_type=jnp.float32)

    weight_term = z_t_dot(z_high, dh_high) + (z_t_dot(z_high, dh_low) + z_t_dot(z_low, dh_high))
    bias_term = jnp.sum(dh_quarter, axis=0)
    pad = (-(fin + 1)) % 8
    terms = jnp.concatenate(
        [weight_term, bias_term[None], jnp.zeros((pad, fout), jnp.float32)], axis=0
    )

    weight_t = weight.T
    p_quarter = jnp.dot(dh_high, weight_t, preferred_element_type=jnp.float32) + jnp.dot(
        dh_low, weight_t, preferred_element_type=jnp.float32
    )
    p_high, p_low = split_bf16(p_quarter.reshape(n_row, tile_size, fin))
    g_parts = aggregate(tiles, cols, rows, live, [p_high, p_low], group_rows)
    spread = jnp.broadcast_to(terms.reshape(1, -1), (n_rep, terms.size))
    both = reduce_rep_a2a(jnp.concatenate([g_parts.reshape(n_rep, -1), spread], axis=1))
    grad_features = both[: g_parts.size // n_rep].reshape(-1, fin)
    totals = both[g_parts.size // n_rep :].reshape(terms.shape)

    factor = 1.0 / math.sqrt(node_total)
    grad_weight = totals[:fin] * factor
    grad_bias = totals[fin] * factor
    return (activated.astype(jnp.bfloat16), grad_features.astype(jnp.bfloat16), grad_weight, grad_bias)


def solution(mesh):
    n_row = mesh.shape["row"]
    n_core = 2
    n_z = 8 if n_row % (8 * n_core) == 0 else 1
    fine = Mesh(
        mesh.devices.reshape(n_row // (n_z * n_core), n_z, n_core, mesh.shape["rep"]),
        ("x", "z", "core", "rep"),
    )
    row = ("x", "z", "core")
    in_specs = (
        P((*row, "rep"), None),
        P(),
        P(),
        P((*row, "rep"), None),
        P(row, "rep", None, None, None, None),
        P(row, "rep", None, None),
        P(row, "rep", None, None),
        P(row, "rep", None, None),
    )
    out_specs = (P((*row, "rep"), None), P((*row, "rep"), None), P(), P())
    return jax.shard_map(shards, mesh=fine, in_specs=in_specs, out_specs=out_specs, check_vma=False)
```
